512 devices in a mesh: ax: 64 (over z, y_hi, core), md: 8 (over y_lo, x).
Axes of the slice: x: 4, y: 8 (y_hi: 4, y_lo: 2; y = y_hi * 2 + y_lo), z: 8, core: 2. Of those that a mesh axis runs over, the one named last changes fastest.
Arguments:
- right_side: float32 [1024, 256, 1024], P('ax', None, 'md'), may hold values from -24 to 24
- coupling: float32 [255], replicated, may hold values from 0.3 to 3
- excess: float32 [256], replicated, may hold values from 0.05 to 0.5
- metric: float32 [256], replicated, may hold values from 1e-06 to 0.0001
Outputs:
- pressure: float32 [1024, 256, 1024], P('ax', None, 'md')
The draws below stay inside these ranges and needn't reach their ends.
All inputs are finite; a program needn't handle non-finite values.
Results may differ from the reference program's by a relative error of at most 0.00007.
Values sent between devices are 32-bit elements; how exact they have to be, the bound alone decides.
No kernel may reach another device: no remote copies, remote signals or barrier semaphores. Data moves between devices by JAX's collectives and lax.ppermute only.
A program may use at most 128 MiB of HBM per device.

```python
import math
import jax
import jax.numpy as jnp
from jax import lax

NR = 256
NT = 1024
SWEEPS = 4
NZ = 1024


def levels(stream_key, extent, shards, smallest, high):
    factor_of, own = 1.0, jax.random.fold_in(stream_key, 6)
    for dim, blocks in shards:
        steps = jnp.exp(jax.random.uniform(jax.random.fold_in(own, dim), (blocks,), jnp.float32, smallest / len(shards), high / len(shards)))
        factor_of = factor_of * jnp.repeat(steps, extent[dim] // blocks).reshape([-1 if axis == dim else 1 for axis in range(len(extent))])
    return factor_of


def gaussian(own_key, dims, width, bound, shards=(), kind=jnp.bfloat16):
    gain = levels(own_key, dims, shards, -0.22, 0.18) if shards else 1.0
    values = jax.random.normal(own_key, dims, jnp.float32) * width * gain
    return jnp.minimum(jnp.maximum(values, -bound), bound).astype(kind)


def setup_inputs(seed: int = 0) -> dict:
    key_list = jax.random.split(jax.random.key(seed), 5)
    right_side = gaussian(key_list[0], (NZ, NR, NT), 4.0, 24.0, ((0, 64), (2, 8)), jnp.float32)
    coupling = jnp.clip(jnp.exp(jax.random.uniform(key_list[1], (NR - 1,), jnp.float32, math.log(0.3), math.log(3.0))), 0.3, 3.0)
    excess = jnp.clip(jnp.exp(jax.random.uniform(key_list[2], (NR,), jnp.float32, math.log(0.05), math.log(0.5))), 0.05, 0.5)
    metric = jnp.clip(jnp.exp(jax.random.uniform(key_list[3], (NR,), jnp.float32, math.log(9.999999974752427e-07), math.log(0.0001))), 9.999999974752427e-07, 0.0001)
    return {"right_side": right_side, "coupling": coupling, "excess": excess, "metric": metric}


def fourier_table(points):
    row_index = jnp.arange(points, dtype=jnp.int32)[:, None]
    col_index = jnp.arange(points, dtype=jnp.int32)[None, :]
    middle = points // 2
    wavenumber = jnp.where(col_index <= middle, col_index, col_index - middle)
    phases = row_index * wavenumber % points
    angles = 2.0 * math.pi / points * phases.astype(jnp.float32)
    weights = jnp.where((col_index == 0) | (col_index == middle), jnp.float32(1.0 / points), jnp.float32(2.0 / points))
    basis_table = jnp.where(col_index <= middle, jnp.cos(angles), jnp.sin(angles))
    return basis_table * jnp.sqrt(weights)

def wave_numbers(count, offset, points):
    positions = offset + jnp.arange(count, dtype=jnp.int32)
    middle = points // 2
    return jnp.where(positions <= middle, positions, positions - middle).astype(jnp.float32)

def links(coupling):
    zero_one = jnp.zeros((1,), coupling.dtype)
    return (jnp.concatenate([zero_one, coupling]), jnp.concatenate([coupling, zero_one]))

def bounds(lower_link, upper_link, excess, metric, wavenumber):
    squared = wavenumber * wavenumber
    radial_floor = excess[:, None] + metric[:, None] * squared[None, :]
    lowest = lax.optimization_barrier(jnp.min(radial_floor, axis=0))
    highest = lax.optimization_barrier(jnp.max(radial_floor + 2.0 * (lower_link + upper_link)[:, None], axis=0)) + 16.0 / 3.0
    return ((highest + lowest) / 2.0, (highest - lowest) / 2.0)

def diagonal_terms(lower_here, upper_here, excess_here, metric_here, wavenumber):
    squared = wavenumber * wavenumber
    return (lower_here + upper_here + excess_here)[:, None] + metric_here[:, None] * squared[None, :] + 2.5

def apply_operator(direction, diagonal, lower_here, upper_here):
    axial_padded = jnp.pad(direction, ((2, 2), (0, 0), (0, 0)))
    radial_padded = jnp.pad(direction, ((0, 0), (1, 1), (0, 0)))
    axial = 4.0 / 3.0 * (axial_padded[1:-3] + axial_padded[3:-1]) - 1.0 / 12.0 * (axial_padded[:-4] + axial_padded[4:])
    radial = lower_here[:, None] * radial_padded[:, :-2] + upper_here[:, None] * radial_padded[:, 2:]
    return diagonal * direction - radial - axial

def chebyshev(source, diagonal, lower_here, upper_here, center, spread):
    ratio_bound = center / spread
    solution = jnp.zeros_like(source)
    residual = source
    direction = source / center
    factor = 1.0 / ratio_bound
    for sweep_index in range(SWEEPS):
        solution = solution + direction
        residual = residual - apply_operator(direction, diagonal, lower_here, upper_here)
        renewed = 1.0 / (2.0 * ratio_bound - factor)
        direction = renewed * factor * direction + 2.0 * renewed / spread * residual
        factor = renewed
    return solution + direction

def reference(right_side, coupling, excess, metric):
    planes, radii, points = right_side.shape
    basis_table = fourier_table(points)
    spectral = jnp.dot(right_side.reshape(-1, points), basis_table, precision=lax.Precision.HIGHEST, preferred_element_type=jnp.float32).reshape(planes, radii, points)
    lower_link, upper_link = links(coupling)
    wavenumber = wave_numbers(points, 0, points)
    center, spread = bounds(lower_link, upper_link, excess, metric, wavenumber)
    diagonal = diagonal_terms(lower_link, upper_link, excess, metric, wavenumber)
    solution = chebyshev(spectral, diagonal, lower_link, upper_link, center, spread)
    pressure = jnp.dot(solution.reshape(-1, points), basis_table.T, precision=lax.Precision.HIGHEST, preferred_element_type=jnp.float32)
    return pressure.reshape(planes, radii, points)
```

```python
import math

import jax
import jax.numpy as jnp
from jax import lax
from jax.sharding import PartitionSpec as P

SWEEPS = 4


def with_halo(value, sides, width):
    for axis, dim in sides:
        size, length = (lax.axis_size(axis), value.shape[dim])
        up = [(i, (i + 1) % size) for i in range(size - 1)]
        down = [(j, i) for i, j in up]
        last = lax.slice_in_dim(value, length - width, length, axis=dim)
        leading = lax.slice_in_dim(value, 0, width, axis=dim)
        before = lax.ppermute(last, axis, up)
        after = lax.ppermute(leading, axis, down)
        value = jnp.concatenate([before, value, after], axis=dim)
    return value


def fourier_table(points):
    split = 32
    col_index = jnp.arange(points, dtype=jnp.int32)[None, :]
    middle = points // 2
    wavenumber = jnp.where(col_index <= middle, col_index, col_index - middle)
    scale = 2.0 * math.pi / points
    coarse = jnp.arange(points // split, dtype=jnp.int32)[:, None] * split
    fine = jnp.arange(split, dtype=jnp.int32)[:, None]
    coarse_angle = scale * ((coarse * wavenumber) % points).astype(jnp.float32)
    fine_angle = scale * ((fine * wavenumber) % points).astype(jnp.float32)
    ca, sa = jnp.cos(coarse_angle)[:, None, :], jnp.sin(coarse_angle)[:, None, :]
    cb, sb = jnp.cos(fine_angle)[None, :, :], jnp.sin(fine_angle)[None, :, :]
    weights = jnp.where(
        (col_index == 0) | (col_index == middle),
        jnp.float32(1.0 / points),
        jnp.float32(2.0 / points),
    )
    cosine = ca * cb - sa * sb
    sine = sa * cb + ca * sb
    basis_table = jnp.where(col_index[None] <= middle, cosine, sine).reshape(points, points)
    return lax.optimization_barrier(basis_table * jnp.sqrt(weights))


def wave_numbers(count, points):
    positions = jnp.arange(count, dtype=jnp.int32)
    middle = points // 2
    return jnp.where(positions <= middle, positions, positions - middle).astype(jnp.float32)


def links(coupling):
    zero_one = jnp.zeros((1,), coupling.dtype)
    return (jnp.concatenate([zero_one, coupling]), jnp.concatenate([coupling, zero_one]))


def bounds(lower_link, upper_link, excess, metric, wavenumber):
    squared = wavenumber * wavenumber
    radial_floor = excess[:, None] + metric[:, None] * squared[None, :]
    lowest = jnp.min(radial_floor, axis=0)
    highest = jnp.max(radial_floor + 2.0 * (lower_link + upper_link)[:, None], axis=0) + 16.0 / 3.0
    return ((highest + lowest) / 2.0, (highest - lowest) / 2.0)


def diagonal_terms(lower_here, upper_here, excess_here, metric_here, wavenumber):
    squared = wavenumber * wavenumber
    return (
        (lower_here + upper_here + excess_here)[:, None]
        + metric_here[:, None] * squared[None, :]
        + 2.5
    )


def apply_grid(direction, diagonal, lower_here, upper_here):
    axial_padded = with_halo(direction, (("ax", 0),), 2)
    radial_padded = with_halo(direction, (("md", 1),), 1)
    axial = 4.0 / 3.0 * (axial_padded[1:-3] + axial_padded[3:-1]) - 1.0 / 12.0 * (
        axial_padded[:-4] + axial_padded[4:]
    )
    radial = (
        lower_here[:, None] * radial_padded[:, :-2] + upper_here[:, None] * radial_padded[:, 2:]
    )
    return diagonal * direction - radial - axial


def chebyshev(source, operate, center, spread):
    ratio_bound = center / spread
    solution = jnp.zeros_like(source)
    residual = source
    direction = source / center
    factor = 1.0 / ratio_bound
    for sweep_index in range(SWEEPS):
        solution = solution + direction
        residual = residual - operate(direction)
        renewed = 1.0 / (2.0 * ratio_bound - factor)
        direction = renewed * factor * direction + 2.0 * renewed / spread * residual
        factor = renewed
    return solution + direction


def per_device(right_side, coupling, excess, metric):
    planes, radii, local_points = right_side.shape
    group_size = lax.axis_size("md")
    points = local_points * group_size
    local_radii = radii // group_size
    basis_table = fourier_table(points)
    lower_link, upper_link = links(coupling)
    gridded = lax.all_to_all(
        right_side.reshape(planes, group_size, local_radii, local_points),
        "md",
        split_axis=1,
        concat_axis=1,
        tiled=True,
    )
    spectral = jnp.dot(
        gridded.transpose(0, 2, 1, 3).reshape(planes * local_radii, points),
        basis_table,
        precision=lax.Precision.HIGHEST,
        preferred_element_type=jnp.float32,
    ).reshape(planes, local_radii, points)
    wavenumber = wave_numbers(points, points)
    offset = lax.axis_index("md") * local_radii
    lower_here = lax.dynamic_slice_in_dim(lower_link, offset, local_radii)
    upper_here = lax.dynamic_slice_in_dim(upper_link, offset, local_radii)
    excess_here = lax.dynamic_slice_in_dim(excess, offset, local_radii)
    metric_here = lax.dynamic_slice_in_dim(metric, offset, local_radii)
    center, spread = bounds(lower_link, upper_link, excess, metric, wavenumber)
    diagonal = diagonal_terms(lower_here, upper_here, excess_here, metric_here, wavenumber)

    def operate(direction):
        return apply_grid(direction, diagonal, lower_here, upper_here)

    solution = chebyshev(spectral, operate, center, spread)
    solved = jnp.dot(
        solution.reshape(planes * local_radii, points),
        basis_table.T,
        precision=lax.Precision.HIGHEST,
        preferred_element_type=jnp.float32,
    ).reshape(planes, local_radii, group_size, local_points).transpose(0, 2, 1, 3)
    returned = lax.all_to_all(solved, "md", split_axis=1, concat_axis=1, tiled=True)
    return returned.reshape(planes, radii, local_points)


def solution(mesh):
    return jax.shard_map(
        per_device,
        mesh=mesh,
        in_specs=(P("ax", None, "md"), P(), P(), P()),
        out_specs=P("ax", None, "md"),
        check_vma=False,
    )
```

```python
import math

import jax
import jax.numpy as jnp
from jax import lax
from jax.sharding import PartitionSpec as P

SWEEPS = 4


def with_halo(value, sides, width):
    for axis, dim in sides:
        size, length = (lax.axis_size(axis), value.shape[dim])
        up = [(i, (i + 1) % size) for i in range(size - 1)]
        down = [(j, i) for i, j in up]
        last = lax.slice_in_dim(value, length - width, length, axis=dim)
        leading = lax.slice_in_dim(value, 0, width, axis=dim)
        before = lax.ppermute(last, axis, up)
        after = lax.ppermute(leading, axis, down)
        value = jnp.concatenate([before, value, after], axis=dim)
    return value


def fourier_table(points):
    split = 32
    col_index = jnp.arange(points, dtype=jnp.int32)[None, :]
    middle = points // 2
    wavenumber = jnp.where(col_index <= middle, col_index, col_index - middle)
    scale = 2.0 * math.pi / points
    coarse = jnp.arange(points // split, dtype=jnp.int32)[:, None] * split
    fine = jnp.arange(split, dtype=jnp.int32)[:, None]
    coarse_angle = scale * ((coarse * wavenumber) % points).astype(jnp.float32)
    fine_angle = scale * ((fine * wavenumber) % points).astype(jnp.float32)
    ca, sa = jnp.cos(coarse_angle)[:, None, :], jnp.sin(coarse_angle)[:, None, :]
    cb, sb = jnp.cos(fine_angle)[None, :, :], jnp.sin(fine_angle)[None, :, :]
    weights = jnp.where(
        (col_index == 0) | (col_index == middle),
        jnp.float32(1.0 / points),
        jnp.float32(2.0 / points),
    )
    cosine = ca * cb - sa * sb
    sine = sa * cb + ca * sb
    basis_table = jnp.where(col_index[None] <= middle, cosine, sine).reshape(points, points)
    return lax.optimization_barrier(basis_table * jnp.sqrt(weights))


def wave_numbers(count, points):
    positions = jnp.arange(count, dtype=jnp.int32)
    middle = points // 2
    return jnp.where(positions <= middle, positions, positions - middle).astype(jnp.float32)


def links(coupling):
    zero_one = jnp.zeros((1,), coupling.dtype)
    return (jnp.concatenate([zero_one, coupling]), jnp.concatenate([coupling, zero_one]))


def bounds(lower_link, upper_link, excess, metric, wavenumber):
    squared = wavenumber * wavenumber
    radial_floor = excess[:, None] + metric[:, None] * squared[None, :]
    lowest = jnp.min(radial_floor, axis=0)
    highest = jnp.max(radial_floor + 2.0 * (lower_link + upper_link)[:, None], axis=0) + 16.0 / 3.0
    return ((highest + lowest) / 2.0, (highest - lowest) / 2.0)


def diagonal_terms(lower_here, upper_here, excess_here, metric_here, wavenumber):
    squared = wavenumber * wavenumber
    return (
        (lower_here + upper_here + excess_here)[:, None]
        + metric_here[:, None] * squared[None, :]
        + 2.5
    )


def apply_inner(direction, diagonal, lower_here, upper_here):
    middle = direction[2:-2, 1:-1]
    axial = 4.0 / 3.0 * (direction[1:-3, 1:-1] + direction[3:-1, 1:-1]) - 1.0 / 12.0 * (
        direction[:-4, 1:-1] + direction[4:, 1:-1]
    )
    radial = (
        lower_here[:, None] * direction[2:-2, :-2] + upper_here[:, None] * direction[2:-2, 2:]
    )
    return diagonal * middle - radial - axial


def chebyshev(source, coefficients, inside, center, spread):
    diagonal, lower_here, upper_here = coefficients
    ratio_bound = center / spread
    solution = jnp.zeros_like(source)
    residual = source
    direction = source / center
    factor = 1.0 / ratio_bound
    for sweep_index in range(1, SWEEPS + 1):
        solution = solution + direction
        cut = slice(sweep_index, diagonal.shape[0] - sweep_index)
        applied = apply_inner(direction, diagonal[cut], lower_here[cut], upper_here[cut])
        solution = solution[2:-2, 1:-1]
        direction = direction[2:-2, 1:-1]
        mask = inside[2 * sweep_index : inside.shape[0] - 2 * sweep_index, cut]
        residual = (residual[2:-2, 1:-1] - applied) * mask
        renewed = 1.0 / (2.0 * ratio_bound - factor)
        direction = renewed * factor * direction + 2.0 * renewed / spread * residual
        factor = renewed
    return solution + direction


def per_device(right_side, coupling, excess, metric):
    planes, radii, local_points = right_side.shape
    group_size = lax.axis_size("md")
    points = local_points * group_size
    local_radii = radii // group_size
    basis_table = fourier_table(points)
    lower_link, upper_link = links(coupling)
    gridded = lax.all_to_all(
        right_side.reshape(planes, group_size, local_radii, local_points),
        "md",
        split_axis=1,
        concat_axis=1,
        tiled=True,
    )
    spectral = jnp.dot(
        gridded.transpose(0, 2, 1, 3).reshape(planes * local_radii, points),
        basis_table,
        precision=lax.Precision.HIGHEST,
        preferred_element_type=jnp.float32,
    ).reshape(planes, local_radii, points)
    wavenumber = wave_numbers(points, points)
    plane_halo, radius_halo = 2 * SWEEPS, SWEEPS
    extended = with_halo(spectral, (("ax", 0),), plane_halo)
    extended = with_halo(extended, (("md", 1),), radius_halo)
    wide_radii = local_radii + 2 * radius_halo
    offset = lax.axis_index("md") * local_radii

    def around(values):
        padded = jnp.pad(values, (radius_halo, radius_halo + radii - values.shape[0]))
        return lax.dynamic_slice_in_dim(padded, offset, wide_radii)

    lower_here, upper_here = around(lower_link), around(upper_link)
    excess_here, metric_here = around(excess), around(metric)
    center, spread = bounds(lower_link, upper_link, excess, metric, wavenumber)
    diagonal = diagonal_terms(lower_here, upper_here, excess_here, metric_here, wavenumber)
    all_planes = planes * lax.axis_size("ax")
    plane_at = lax.axis_index("ax") * planes - plane_halo + jnp.arange(planes + 2 * plane_halo)
    radius_at = offset - radius_halo + jnp.arange(wide_radii)
    inside = (
        ((plane_at >= 0) & (plane_at < all_planes))[:, None]
        & ((radius_at >= 0) & (radius_at < radii))[None, :]
    ).astype(jnp.float32)[:, :, None]
    solution = chebyshev(extended, (diagonal, lower_here, upper_here), inside, center, spread)
    solved = jnp.dot(
        solution.reshape(planes * local_radii, points),
        basis_table.T,
        precision=lax.Precision.HIGHEST,
        preferred_element_type=jnp.float32,
    ).reshape(planes, local_radii, group_size, local_points).transpose(0, 2, 1, 3)
    returned = lax.all_to_all(solved, "md", split_axis=1, concat_axis=1, tiled=True)
    return returned.reshape(planes, radii, local_points)


def solution(mesh):
    return jax.shard_map(
        per_device,
        mesh=mesh,
        in_specs=(P("ax", None, "md"), P(), P(), P()),
        out_specs=P("ax", None, "md"),
        check_vma=False,
    )
```

```python
import math

import jax
import jax.numpy as jnp
from jax import lax
from jax.sharding import PartitionSpec as P

SWEEPS = 4


def with_halo(value, sides, width):
    for axis, dim in sides:
        size, length = (lax.axis_size(axis), value.shape[dim])
        up = [(i, (i + 1) % size) for i in range(size - 1)]
        down = [(j, i) for i, j in up]
        last = lax.slice_in_dim(value, length - width, length, axis=dim)
        leading = lax.slice_in_dim(value, 0, width, axis=dim)
        before = lax.ppermute(last, axis, up)
        after = lax.ppermute(leading, axis, down)
        value = jnp.concatenate([before, value, after], axis=dim)
    return value


def fourier_table(points):
    split = 32
    col_index = jnp.arange(points, dtype=jnp.int32)[None, :]
    middle = points // 2
    wavenumber = jnp.where(col_index <= middle, col_index, col_index - middle)
    scale = 2.0 * math.pi / points
    coarse = jnp.arange(points // split, dtype=jnp.int32)[:, None] * split
    fine = jnp.arange(split, dtype=jnp.int32)[:, None]
    coarse_angle = scale * ((coarse * wavenumber) % points).astype(jnp.float32)
    fine_angle = scale * ((fine * wavenumber) % points).astype(jnp.float32)
    ca, sa = jnp.cos(coarse_angle)[:, None, :], jnp.sin(coarse_angle)[:, None, :]
    cb, sb = jnp.cos(fine_angle)[None, :, :], jnp.sin(fine_angle)[None, :, :]
    weights = jnp.where(
        (col_index == 0) | (col_index == middle),
        jnp.float32(1.0 / points),
        jnp.float32(2.0 / points),
    )
    cosine = ca * cb - sa * sb
    sine = sa * cb + ca * sb
    basis_table = jnp.where(col_index[None] <= middle, cosine, sine).reshape(points, points)
    return lax.optimization_barrier(basis_table * jnp.sqrt(weights))


def wave_numbers(count, points):
    positions = jnp.arange(count, dtype=jnp.int32)
    middle = points // 2
    return jnp.where(positions <= middle, positions, positions - middle).astype(jnp.float32)


def links(coupling):
    zero_one = jnp.zeros((1,), coupling.dtype)
    return (jnp.concatenate([zero_one, coupling]), jnp.concatenate([coupling, zero_one]))


def bounds(lower_link, upper_link, excess, metric, wavenumber):
    squared = wavenumber * wavenumber
    radial_floor = excess[:, None] + metric[:, None] * squared[None, :]
    lowest = jnp.min(radial_floor, axis=0)
    highest = jnp.max(radial_floor + 2.0 * (lower_link + upper_link)[:, None], axis=0) + 16.0 / 3.0
    return ((highest + lowest) / 2.0, (highest - lowest) / 2.0)


def diagonal_terms(lower_here, upper_here, excess_here, metric_here, wavenumber):
    squared = wavenumber * wavenumber
    return (
        (lower_here + upper_here + excess_here)[:, None]
        + metric_here[:, None] * squared[None, :]
        + 2.5
    )


def apply_inner(direction, diagonal, lower_here, upper_here):
    middle = direction[2:-2, 1:-1]
    axial = 4.0 / 3.0 * (direction[1:-3, 1:-1] + direction[3:-1, 1:-1]) - 1.0 / 12.0 * (
        direction[:-4, 1:-1] + direction[4:, 1:-1]
    )
    radial = (
        lower_here[:, None] * direction[2:-2, :-2] + upper_here[:, None] * direction[2:-2, 2:]
    )
    return diagonal * middle - radial - axial


def chebyshev(source, coefficients, inside, center, spread):
    diagonal, lower_here, upper_here = coefficients
    ratio_bound = center / spread
    solution = jnp.zeros_like(source)
    residual = source
    direction = source / center
    factor = 1.0 / ratio_bound
    for sweep_index in range(1, SWEEPS + 1):
        solution = solution + direction
        cut = slice(sweep_index, diagonal.shape[0] - sweep_index)
        applied = apply_inner(direction, diagonal[cut], lower_here[cut], upper_here[cut])
        solution = solution[2:-2, 1:-1]
        direction = direction[2:-2, 1:-1]
        mask = inside[2 * sweep_index : inside.shape[0] - 2 * sweep_index, cut]
        residual = (residual[2:-2, 1:-1] - applied) * mask
        renewed = 1.0 / (2.0 * ratio_bound - factor)
        direction = renewed * factor * direction + 2.0 * renewed / spread * residual
        factor = renewed
    return solution + direction


def blocks_in(right_side, basis_table):
    planes, radii, local_points = right_side.shape
    group_size = lax.axis_size("md")
    local_radii = radii // group_size
    here = lax.axis_index("md")
    spectral = None
    for shift in range(group_size):
        target = (here + shift) % group_size
        block = lax.dynamic_slice_in_dim(right_side, target * local_radii, local_radii, axis=1)
        if shift:
            pairs = [(i, (i + shift) % group_size) for i in range(group_size)]
            block = lax.ppermute(block, "md", pairs)
        source = (here - shift) % group_size
        rows = lax.dynamic_slice_in_dim(basis_table, source * local_points, local_points)
        part = jnp.dot(
            block.reshape(planes * local_radii, local_points),
            rows,
            precision=lax.Precision.HIGHEST,
            preferred_element_type=jnp.float32,
        )
        spectral = part if spectral is None else spectral + part
    return spectral.reshape(planes, local_radii, -1)


def blocks_out(solution, basis_table, radii):
    planes, local_radii, points = solution.shape
    group_size = lax.axis_size("md")
    local_points = points // group_size
    here = lax.axis_index("md")
    flat = solution.reshape(planes * local_radii, points)
    pressure = jnp.zeros((planes, radii, local_points), jnp.float32)
    for shift in range(group_size):
        target = (here + shift) % group_size
        rows = lax.dynamic_slice_in_dim(basis_table, target * local_points, local_points)
        block = lax.dot_general(
            flat,
            rows,
            (((1,), (1,)), ((), ())),
            precision=lax.Precision.HIGHEST,
            preferred_element_type=jnp.float32,
        ).reshape(planes, local_radii, local_points)
        if shift:
            pairs = [(i, (i + shift) % group_size) for i in range(group_size)]
            block = lax.ppermute(block, "md", pairs)
        source = (here - shift) % group_size
        pressure = lax.dynamic_update_slice_in_dim(pressure, block, source * local_radii, axis=1)
    return pressure


def per_device(right_side, coupling, excess, metric):
    planes, radii, local_points = right_side.shape
    group_size = lax.axis_size("md")
    points = local_points * group_size
    local_radii = radii // group_size
    basis_table = fourier_table(points)
    lower_link, upper_link = links(coupling)
    spectral = blocks_in(right_side, basis_table)
    wavenumber = wave_numbers(points, points)
    plane_halo, radius_halo = 2 * SWEEPS, SWEEPS
    extended = with_halo(spectral, (("ax", 0),), plane_halo)
    extended = with_halo(extended, (("md", 1),), radius_halo)
    wide_radii = local_radii + 2 * radius_halo
    offset = lax.axis_index("md") * local_radii

    def around(values):
        padded = jnp.pad(values, (radius_halo, radius_halo + radii - values.shape[0]))
        return lax.dynamic_slice_in_dim(padded, offset, wide_radii)

    lower_here, upper_here = around(lower_link), around(upper_link)
    excess_here, metric_here = around(excess), around(metric)
    center, spread = bounds(lower_link, upper_link, excess, metric, wavenumber)
    diagonal = diagonal_terms(lower_here, upper_here, excess_here, metric_here, wavenumber)
    all_planes = planes * lax.axis_size("ax")
    plane_at = lax.axis_index("ax") * planes - plane_halo + jnp.arange(planes + 2 * plane_halo)
    radius_at = offset - radius_halo + jnp.arange(wide_radii)
    inside = (
        ((plane_at >= 0) & (plane_at < all_planes))[:, None]
        & ((radius_at >= 0) & (radius_at < radii))[None, :]
    ).astype(jnp.float32)[:, :, None]
    solution = chebyshev(extended, (diagonal, lower_here, upper_here), inside, center, spread)
    return blocks_out(solution, basis_table, radii)


def solution(mesh):
    return jax.shard_map(
        per_device,
        mesh=mesh,
        in_specs=(P("ax", None, "md"), P(), P(), P()),
        out_specs=P("ax", None, "md"),
        check_vma=False,
    )
```

```python
import math

import jax
import jax.numpy as jnp
from jax import lax
from jax.sharding import PartitionSpec as P

SWEEPS = 4


def with_halo(value, sides, width):
    for axis, dim in sides:
        size, length = (lax.axis_size(axis), value.shape[dim])
        up = [(i, (i + 1) % size) for i in range(size - 1)]
        down = [(j, i) for i, j in up]
        last = lax.slice_in_dim(value, length - width, length, axis=dim)
        leading = lax.slice_in_dim(value, 0, width, axis=dim)
        before = lax.ppermute(last, axis, up)
        after = lax.ppermute(leading, axis, down)
        value = jnp.concatenate([before, value, after], axis=dim)
    return value


def fourier_table(points):
    split = 32
    col_index = jnp.arange(points, dtype=jnp.int32)[None, :]
    middle = points // 2
    wavenumber = jnp.where(col_index <= middle, col_index, col_index - middle)
    scale = 2.0 * math.pi / points
    coarse = jnp.arange(points // split, dtype=jnp.int32)[:, None] * split
    fine = jnp.arange(split, dtype=jnp.int32)[:, None]
    coarse_angle = scale * ((coarse * wavenumber) % points).astype(jnp.float32)
    fine_angle = scale * ((fine * wavenumber) % points).astype(jnp.float32)
    ca, sa = jnp.cos(coarse_angle)[:, None, :], jnp.sin(coarse_angle)[:, None, :]
    cb, sb = jnp.cos(fine_angle)[None, :, :], jnp.sin(fine_angle)[None, :, :]
    weights = jnp.where(
        (col_index == 0) | (col_index == middle),
        jnp.float32(1.0 / points),
        jnp.float32(2.0 / points),
    )
    cosine = ca * cb - sa * sb
    sine = sa * cb + ca * sb
    basis_table = jnp.where(col_index[None] <= middle, cosine, sine).reshape(points, points)
    return lax.optimization_barrier(basis_table * jnp.sqrt(weights))


def wave_numbers(count, points):
    positions = jnp.arange(count, dtype=jnp.int32)
    middle = points // 2
    return jnp.where(positions <= middle, positions, positions - middle).astype(jnp.float32)


def links(coupling):
    zero_one = jnp.zeros((1,), coupling.dtype)
    return (jnp.concatenate([zero_one, coupling]), jnp.concatenate([coupling, zero_one]))


def bounds(lower_link, upper_link, excess, metric, wavenumber):
    squared = wavenumber * wavenumber
    radial_floor = excess[:, None] + metric[:, None] * squared[None, :]
    lowest = jnp.min(radial_floor, axis=0)
    highest = jnp.max(radial_floor + 2.0 * (lower_link + upper_link)[:, None], axis=0) + 16.0 / 3.0
    return ((highest + lowest) / 2.0, (highest - lowest) / 2.0)


def diagonal_terms(lower_here, upper_here, excess_here, metric_here, wavenumber):
    squared = wavenumber * wavenumber
    return (
        (lower_here + upper_here + excess_here)[:, None]
        + metric_here[:, None] * squared[None, :]
        + 2.5
    )


def apply_inner(direction, diagonal, lower_here, upper_here):
    middle = direction[2:-2, 1:-1]
    axial = 4.0 / 3.0 * (direction[1:-3, 1:-1] + direction[3:-1, 1:-1]) - 1.0 / 12.0 * (
        direction[:-4, 1:-1] + direction[4:, 1:-1]
    )
    radial = lower_here * direction[2:-2, :-2] + upper_here * direction[2:-2, 2:]
    return diagonal * middle - radial - axial


def chebyshev(source, coefficients, inside, center, spread):
    diagonal, lower_here, upper_here = coefficients
    ratio_bound = center / spread
    solution = jnp.zeros_like(source)
    residual = source
    direction = source / center
    factor = 1.0 / ratio_bound
    for sweep_index in range(1, SWEEPS + 1):
        solution = solution + direction
        cut = slice(sweep_index, diagonal.shape[0] - sweep_index)
        applied = apply_inner(direction, diagonal[cut], lower_here[cut], upper_here[cut])
        solution = solution[2:-2, 1:-1]
        direction = direction[2:-2, 1:-1]
        mask = inside[2 * sweep_index : inside.shape[0] - 2 * sweep_index, cut]
        residual = (residual[2:-2, 1:-1] - applied) * mask
        renewed = 1.0 / (2.0 * ratio_bound - factor)
        direction = renewed * factor * direction + 2.0 * renewed / spread * residual
        factor = renewed
    return solution + direction


def per_device(right_side, coupling, excess, metric):
    planes, radii, local_points = right_side.shape
    group_size = lax.axis_size("md")
    points = local_points * group_size
    local_radii = radii // group_size
    basis_table = fourier_table(points)
    lower_link, upper_link = links(coupling)
    gridded = lax.all_to_all(
        right_side.reshape(planes, group_size, local_radii, local_points),
        "md",
        split_axis=1,
        concat_axis=1,
        tiled=True,
    )
    spectral = jnp.dot(
        gridded.transpose(0, 2, 1, 3).reshape(planes * local_radii, points),
        basis_table,
        precision=lax.Precision.HIGH,
        preferred_element_type=jnp.float32,
    ).reshape(planes, local_radii, points)
    wavenumber = wave_numbers(points, points)
    fold = (points // 128, 128)
    spectral = spectral.reshape(planes, local_radii, *fold)
    plane_halo, radius_halo = 2 * SWEEPS, SWEEPS
    extended = with_halo(spectral, (("ax", 0),), plane_halo)
    extended = with_halo(extended, (("md", 1),), radius_halo)
    wide_radii = local_radii + 2 * radius_halo
    offset = lax.axis_index("md") * local_radii

    def around(values):
        padded = jnp.pad(values, (radius_halo, radius_halo + radii - values.shape[0]))
        return lax.dynamic_slice_in_dim(padded, offset, wide_radii)

    lower_here, upper_here = around(lower_link), around(upper_link)
    excess_here, metric_here = around(excess), around(metric)
    center, spread = bounds(lower_link, upper_link, excess, metric, wavenumber)
    diagonal = diagonal_terms(lower_here, upper_here, excess_here, metric_here, wavenumber)
    all_planes = planes * lax.axis_size("ax")
    plane_at = lax.axis_index("ax") * planes - plane_halo + jnp.arange(planes + 2 * plane_halo)
    radius_at = offset - radius_halo + jnp.arange(wide_radii)
    inside = (
        ((plane_at >= 0) & (plane_at < all_planes))[:, None]
        & ((radius_at >= 0) & (radius_at < radii))[None, :]
    ).astype(jnp.float32)[:, :, None, None]
    coefficients = (
        diagonal.reshape(wide_radii, *fold),
        lower_here[:, None, None],
        upper_here[:, None, None],
    )
    solution = chebyshev(
        extended, coefficients, inside, center.reshape(fold), spread.reshape(fold)
    )
    solved = jnp.dot(
        solution.reshape(planes * local_radii, points),
        basis_table.T,
        precision=lax.Precision.HIGH,
        preferred_element_type=jnp.float32,
    ).reshape(planes, local_radii, group_size, local_points).transpose(0, 2, 1, 3)
    returned = lax.all_to_all(solved, "md", split_axis=1, concat_axis=1, tiled=True)
    return returned.reshape(planes, radii, local_points)


def solution(mesh):
    return jax.shard_map(
        per_device,
        mesh=mesh,
        in_specs=(P("ax", None, "md"), P(), P(), P()),
        out_specs=P("ax", None, "md"),
        check_vma=False,
    )
```

```python
import math

import jax
import jax.numpy as jnp
from jax import lax
from jax.sharding import PartitionSpec as P

SWEEPS = 4


def with_halo(value, sides, width):
    for axis, dim in sides:
        size, length = (lax.axis_size(axis), value.shape[dim])
        up = [(i, (i + 1) % size) for i in range(size - 1)]
        down = [(j, i) for i, j in up]
        last = lax.slice_in_dim(value, length - width, length, axis=dim)
        leading = lax.slice_in_dim(value, 0, width, axis=dim)
        before = lax.ppermute(last, axis, up)
        after = lax.ppermute(leading, axis, down)
        value = jnp.concatenate([before, value, after], axis=dim)
    return value


def fourier_table(points):
    split = 32
    col_index = jnp.arange(points, dtype=jnp.int32)[None, :]
    middle = points // 2
    wavenumber = jnp.where(col_index <= middle, col_index, col_index - middle)
    scale = 2.0 * math.pi / points
    coarse = jnp.arange(points // split, dtype=jnp.int32)[:, None] * split
    fine = jnp.arange(split, dtype=jnp.int32)[:, None]
    coarse_angle = scale * ((coarse * wavenumber) % points).astype(jnp.float32)
    fine_angle = scale * ((fine * wavenumber) % points).astype(jnp.float32)
    ca, sa = jnp.cos(coarse_angle)[:, None, :], jnp.sin(coarse_angle)[:, None, :]
    cb, sb = jnp.cos(fine_angle)[None, :, :], jnp.sin(fine_angle)[None, :, :]
    weights = jnp.where(
        (col_index == 0) | (col_index == middle),
        jnp.float32(1.0 / points),
        jnp.float32(2.0 / points),
    )
    cosine = ca * cb - sa * sb
    sine = sa * cb + ca * sb
    basis_table = jnp.where(col_index[None] <= middle, cosine, sine).reshape(points, points)
    return lax.optimization_barrier(basis_table * jnp.sqrt(weights))


def wave_numbers(count, points):
    positions = jnp.arange(count, dtype=jnp.int32)
    middle = points // 2
    return jnp.where(positions <= middle, positions, positions - middle).astype(jnp.float32)


def links(coupling):
    zero_one = jnp.zeros((1,), coupling.dtype)
    return (jnp.concatenate([zero_one, coupling]), jnp.concatenate([coupling, zero_one]))


def bounds(lower_link, upper_link, excess, metric, wavenumber):
    squared = wavenumber * wavenumber
    radial_floor = excess[:, None] + metric[:, None] * squared[None, :]
    lowest = jnp.min(radial_floor, axis=0)
    highest = jnp.max(radial_floor + 2.0 * (lower_link + upper_link)[:, None], axis=0) + 16.0 / 3.0
    return ((highest + lowest) / 2.0, (highest - lowest) / 2.0)


def diagonal_terms(lower_here, upper_here, excess_here, metric_here, wavenumber):
    squared = wavenumber * wavenumber
    return (
        (lower_here + upper_here + excess_here)[:, None]
        + metric_here[:, None] * squared[None, :]
        + 2.5
    )


def apply_inner(direction, diagonal, lower_here, upper_here):
    middle = direction[2:-2, 1:-1]
    axial = 4.0 / 3.0 * (direction[1:-3, 1:-1] + direction[3:-1, 1:-1]) - 1.0 / 12.0 * (
        direction[:-4, 1:-1] + direction[4:, 1:-1]
    )
    radial = lower_here * direction[2:-2, :-2] + upper_here * direction[2:-2, 2:]
    return diagonal * middle - radial - axial


def chebyshev(source, coefficients, inside, center, spread):
    diagonal, lower_here, upper_here = coefficients
    ratio_bound = center / spread
    solution = jnp.zeros_like(source)
    residual = source
    direction = source / center
    factor = 1.0 / ratio_bound
    for sweep_index in range(1, SWEEPS + 1):
        solution = solution + direction
        cut = slice(sweep_index, diagonal.shape[0] - sweep_index)
        applied = apply_inner(direction, diagonal[cut], lower_here[cut], upper_here[cut])
        solution = solution[2:-2, 1:-1]
        direction = direction[2:-2, 1:-1]
        mask = inside[2 * sweep_index : inside.shape[0] - 2 * sweep_index, cut]
        residual = (residual[2:-2, 1:-1] - applied) * mask
        renewed = 1.0 / (2.0 * ratio_bound - factor)
        direction = renewed * factor * direction + 2.0 * renewed / spread * residual
        factor = renewed
    return solution + direction


def per_device(right_side, coupling, excess, metric):
    planes, radii, local_points = right_side.shape
    group_size = lax.axis_size("md")
    points = local_points * group_size
    local_radii = radii // group_size
    basis_table = fourier_table(points)
    lower_link, upper_link = links(coupling)
    gridded = lax.all_to_all(
        right_side.reshape(planes, group_size, local_radii, local_points),
        "md",
        split_axis=1,
        concat_axis=1,
        tiled=True,
    )
    fold = (points // 128, 128)
    spectral = lax.dot_general(
        gridded.transpose(0, 2, 1, 3).reshape(planes * local_radii, points),
        basis_table.reshape(points, *fold),
        (((1,), (0,)), ((), ())),
        precision=lax.Precision.HIGH,
        preferred_element_type=jnp.float32,
    ).reshape(planes, local_radii, *fold)
    wavenumber = wave_numbers(points, points)
    plane_halo, radius_halo = 2 * SWEEPS, SWEEPS
    extended = with_halo(spectral, (("ax", 0),), plane_halo)
    extended = with_halo(extended, (("md", 1),), radius_halo)
    wide_radii = local_radii + 2 * radius_halo
    offset = lax.axis_index("md") * local_radii

    def around(values):
        padded = jnp.pad(values, (radius_halo, radius_halo + radii - values.shape[0]))
        return lax.dynamic_slice_in_dim(padded, offset, wide_radii)

    lower_here, upper_here = around(lower_link), around(upper_link)
    excess_here, metric_here = around(excess), around(metric)
    center, spread = bounds(lower_link, upper_link, excess, metric, wavenumber)
    diagonal = diagonal_terms(lower_here, upper_here, excess_here, metric_here, wavenumber)
    all_planes = planes * lax.axis_size("ax")
    plane_at = lax.axis_index("ax") * planes - plane_halo + jnp.arange(planes + 2 * plane_halo)
    radius_at = offset - radius_halo + jnp.arange(wide_radii)
    inside = (
        ((plane_at >= 0) & (plane_at < all_planes))[:, None]
        & ((radius_at >= 0) & (radius_at < radii))[None, :]
    ).astype(jnp.float32)[:, :, None, None]
    coefficients = (
        diagonal.reshape(wide_radii, *fold),
        lower_here[:, None, None],
        upper_here[:, None, None],
    )
    solution = chebyshev(
        extended, coefficients, inside, center.reshape(fold), spread.reshape(fold)
    )
    solved = lax.dot_general(
        solution.reshape(planes * local_radii, *fold),
        basis_table.reshape(points, *fold),
        (((1, 2), (1, 2)), ((), ())),
        precision=lax.Precision.HIGH,
        preferred_element_type=jnp.float32,
    ).reshape(planes, local_radii, group_size, local_points).transpose(0, 2, 1, 3)
    returned = lax.all_to_all(solved, "md", split_axis=1, concat_axis=1, tiled=True)
    return returned.reshape(planes, radii, local_points)


def solution(mesh):
    return jax.shard_map(
        per_device,
        mesh=mesh,
        in_specs=(P("ax", None, "md"), P(), P(), P()),
        out_specs=P("ax", None, "md"),
        check_vma=False,
    )
```

```python
import math

import jax
import jax.numpy as jnp
from jax import lax
from jax.sharding import PartitionSpec as P


SWEEPS = 4


def deep_halo(value, depth, width):
    def shifted(piece, axis, upward):
        size = lax.axis_size(axis)
        up = [(i, i + 1) for i in range(size - 1)]
        return lax.ppermute(piece, axis, up if upward else [(j, i) for i, j in up])

    below = shifted(value[-depth:], "ax", True)
    above = shifted(value[:depth], "ax", False)
    left = shifted(value[:, -width:], "md", True)
    right = shifted(value[:, :width], "md", False)
    strips = jnp.concatenate([below, above], axis=0)
    corner_left = shifted(strips[:, -width:], "md", True)
    corner_right = shifted(strips[:, :width], "md", False)
    lower = jnp.concatenate([corner_left[:depth], below, corner_right[:depth]], axis=1)
    middle = jnp.concatenate([left, value, right], axis=1)
    upper = jnp.concatenate([corner_left[depth:], above, corner_right[depth:]], axis=1)
    return jnp.concatenate([lower, middle, upper], axis=0)


def fourier_table(points):
    split = 32
    col_index = jnp.arange(points, dtype=jnp.int32)[None, :]
    middle = points // 2
    wavenumber = jnp.where(col_index <= middle, col_index, col_index - middle)
    scale = 2.0 * math.pi / points
    coarse = jnp.arange(points // split, dtype=jnp.int32)[:, None] * split
    fine = jnp.arange(split, dtype=jnp.int32)[:, None]
    coarse_angle = scale * ((coarse * wavenumber) % points).astype(jnp.float32)
    fine_angle = scale * ((fine * wavenumber) % points).astype(jnp.float32)
    ca, sa = jnp.cos(coarse_angle)[:, None, :], jnp.sin(coarse_angle)[:, None, :]
    cb, sb = jnp.cos(fine_angle)[None, :, :], jnp.sin(fine_angle)[None, :, :]
    weights = jnp.where(
        (col_index == 0) | (col_index == middle),
        jnp.float32(1.0 / points),
        jnp.float32(2.0 / points),
    )
    cosine = ca * cb - sa * sb
    sine = sa * cb + ca * sb
    basis_table = jnp.where(col_index[None] <= middle, cosine, sine).reshape(points, points)
    return lax.optimization_barrier(basis_table * jnp.sqrt(weights))


def wave_numbers(count, points):
    positions = jnp.arange(count, dtype=jnp.int32)
    middle = points // 2
    return jnp.where(positions <= middle, positions, positions - middle).astype(jnp.float32)


def links(coupling):
    zero_one = jnp.zeros((1,), coupling.dtype)
    return (jnp.concatenate([zero_one, coupling]), jnp.concatenate([coupling, zero_one]))


def bounds(lower_link, upper_link, excess, metric, wavenumber):
    squared = wavenumber * wavenumber
    radial_floor = excess[:, None] + metric[:, None] * squared[None, :]
    lowest = jnp.min(radial_floor, axis=0)
    highest = jnp.max(radial_floor + 2.0 * (lower_link + upper_link)[:, None], axis=0) + 16.0 / 3.0
    return ((highest + lowest) / 2.0, (highest - lowest) / 2.0)


def diagonal_terms(lower_here, upper_here, excess_here, metric_here, wavenumber):
    squared = wavenumber * wavenumber
    return (
        (lower_here + upper_here + excess_here)[:, None]
        + metric_here[:, None] * squared[None, :]
        + 2.5
    )


def apply_inner(direction, diagonal, lower_here, upper_here):
    middle = direction[2:-2, 1:-1]
    axial = 4.0 / 3.0 * (direction[1:-3, 1:-1] + direction[3:-1, 1:-1]) - 1.0 / 12.0 * (
        direction[:-4, 1:-1] + direction[4:, 1:-1]
    )
    radial = lower_here * direction[2:-2, :-2] + upper_here * direction[2:-2, 2:]
    return diagonal * middle - radial - axial


def chebyshev(source, coefficients, inside, center, spread):
    diagonal, lower_here, upper_here = coefficients
    ratio_bound = center / spread
    solution = jnp.zeros_like(source)
    residual = source
    direction = source / center
    factor = 1.0 / ratio_bound
    for sweep_index in range(1, SWEEPS + 1):
        solution = solution + direction
        cut = slice(sweep_index, diagonal.shape[0] - sweep_index)
        applied = apply_inner(direction, diagonal[cut], lower_here[cut], upper_here[cut])
        solution = solution[2:-2, 1:-1]
        direction = direction[2:-2, 1:-1]
        mask = inside[2 * sweep_index : inside.shape[0] - 2 * sweep_index, cut]
        residual = (residual[2:-2, 1:-1] - applied) * mask
        renewed = 1.0 / (2.0 * ratio_bound - factor)
        direction = renewed * factor * direction + 2.0 * renewed / spread * residual
        factor = renewed
    return solution + direction


def per_device(right_side, coupling, excess, metric):
    planes, radii, local_points = right_side.shape
    group_size = lax.axis_size("md")
    points = local_points * group_size
    local_radii = radii // group_size
    basis_table = fourier_table(points)
    lower_link, upper_link = links(coupling)
    gridded = lax.all_to_all(
        right_side.reshape(planes, group_size, local_radii, local_points),
        "md",
        split_axis=1,
        concat_axis=1,
        tiled=True,
    )
    fold = (points // 128, 128)
    spectral = lax.dot_general(
        gridded.transpose(0, 2, 1, 3).reshape(planes * local_radii, points),
        basis_table.reshape(points, *fold),
        (((1,), (0,)), ((), ())),
        precision=lax.Precision.HIGH,
        preferred_element_type=jnp.float32,
    ).reshape(planes, local_radii, *fold)
    wavenumber = wave_numbers(points, points)
    plane_halo, radius_halo = 2 * SWEEPS, SWEEPS
    extended = deep_halo(spectral, plane_halo, radius_halo)
    wide_radii = local_radii + 2 * radius_halo
    offset = lax.axis_index("md") * local_radii

    def around(values):
        padded = jnp.pad(values, (radius_halo, radius_halo + radii - values.shape[0]))
        return lax.dynamic_slice_in_dim(padded, offset, wide_radii)

    lower_here, upper_here = around(lower_link), around(upper_link)
    excess_here, metric_here = around(excess), around(metric)
    center, spread = bounds(lower_link, upper_link, excess, metric, wavenumber)
    diagonal = diagonal_terms(lower_here, upper_here, excess_here, metric_here, wavenumber)
    all_planes = planes * lax.axis_size("ax")
    plane_at = lax.axis_index("ax") * planes - plane_halo + jnp.arange(planes + 2 * plane_halo)
    radius_at = offset - radius_halo + jnp.arange(wide_radii)
    inside = (
        ((plane_at >= 0) & (plane_at < all_planes))[:, None]
        & ((radius_at >= 0) & (radius_at < radii))[None, :]
    ).astype(jnp.float32)[:, :, None, None]
    coefficients = (
        diagonal.reshape(wide_radii, *fold),
        lower_here[:, None, None],
        upper_here[:, None, None],
    )
    solution = chebyshev(
        extended, coefficients, inside, center.reshape(fold), spread.reshape(fold)
    )
    solved = lax.dot_general(
        solution.reshape(planes * local_radii, *fold),
        basis_table.reshape(points, *fold),
        (((1, 2), (1, 2)), ((), ())),
        precision=lax.Precision.HIGH,
        preferred_element_type=jnp.float32,
    ).reshape(planes, local_radii, group_size, local_points).transpose(0, 2, 1, 3)
    returned = lax.all_to_all(solved, "md", split_axis=1, concat_axis=1, tiled=True)
    return returned.reshape(planes, radii, local_points)


def solution(mesh):
    return jax.shard_map(
        per_device,
        mesh=mesh,
        in_specs=(P("ax", None, "md"), P(), P(), P()),
        out_specs=P("ax", None, "md"),
        check_vma=False,
    )
```

```python
import math

import jax
import jax.numpy as jnp
from jax import lax
from jax.sharding import PartitionSpec as P

SWEEPS = 4


def with_halo(value, sides, width):
    for axis, dim in sides:
        size, length = (lax.axis_size(axis), value.shape[dim])
        up = [(i, (i + 1) % size) for i in range(size - 1)]
        down = [(j, i) for i, j in up]
        last = lax.slice_in_dim(value, length - width, length, axis=dim)
        leading = lax.slice_in_dim(value, 0, width, axis=dim)
        before = lax.ppermute(last, axis, up)
        after = lax.ppermute(leading, axis, down)
        value = jnp.concatenate([before, value, after], axis=dim)
    return value


def fourier_table(points):
    split = 32
    col_index = jnp.arange(points, dtype=jnp.int32)[None, :]
    middle = points // 2
    wavenumber = jnp.where(col_index <= middle, col_index, col_index - middle)
    scale = 2.0 * math.pi / points
    coarse = jnp.arange(points // split, dtype=jnp.int32)[:, None] * split
    fine = jnp.arange(split, dtype=jnp.int32)[:, None]
    coarse_angle = scale * ((coarse * wavenumber) % points).astype(jnp.float32)
    fine_angle = scale * ((fine * wavenumber) % points).astype(jnp.float32)
    ca, sa = jnp.cos(coarse_angle)[:, None, :], jnp.sin(coarse_angle)[:, None, :]
    cb, sb = jnp.cos(fine_angle)[None, :, :], jnp.sin(fine_angle)[None, :, :]
    weights = jnp.where(
        (col_index == 0) | (col_index == middle),
        jnp.float32(1.0 / points),
        jnp.float32(2.0 / points),
    )
    cosine = ca * cb - sa * sb
    sine = sa * cb + ca * sb
    basis_table = jnp.where(col_index[None] <= middle, cosine, sine).reshape(points, points)
    return lax.optimization_barrier(basis_table * jnp.sqrt(weights))


def wave_numbers(count, points):
    positions = jnp.arange(count, dtype=jnp.int32)
    middle = points // 2
    return jnp.where(positions <= middle, positions, positions - middle).astype(jnp.float32)


def links(coupling):
    zero_one = jnp.zeros((1,), coupling.dtype)
    return (jnp.concatenate([zero_one, coupling]), jnp.concatenate([coupling, zero_one]))


def bounds(lower_link, upper_link, excess, metric, wavenumber):
    squared = wavenumber * wavenumber
    radial_floor = excess[:, None] + metric[:, None] * squared[None, :]
    lowest = jnp.min(radial_floor, axis=0)
    highest = jnp.max(radial_floor + 2.0 * (lower_link + upper_link)[:, None], axis=0) + 16.0 / 3.0
    return ((highest + lowest) / 2.0, (highest - lowest) / 2.0)


def diagonal_terms(lower_here, upper_here, excess_here, metric_here, wavenumber):
    squared = wavenumber * wavenumber
    return (
        (lower_here + upper_here + excess_here)[:, None]
        + metric_here[:, None] * squared[None, :]
        + 2.5
    )


def apply_inner(direction, diagonal, lower_here, upper_here):
    middle = direction[2:-2, 1:-1]
    axial = 4.0 / 3.0 * (direction[1:-3, 1:-1] + direction[3:-1, 1:-1]) - 1.0 / 12.0 * (
        direction[:-4, 1:-1] + direction[4:, 1:-1]
    )
    radial = lower_here * direction[2:-2, :-2] + upper_here * direction[2:-2, 2:]
    return diagonal * middle - radial - axial


def chebyshev(source, coefficients, inside, center, spread):
    diagonal, lower_here, upper_here = coefficients
    ratio_bound = center / spread
    solution = jnp.zeros_like(source)
    residual = source
    direction = source / center
    factor = 1.0 / ratio_bound
    for sweep_index in range(1, SWEEPS + 1):
        solution = solution + direction
        cut = slice(sweep_index, diagonal.shape[0] - sweep_index)
        applied = apply_inner(direction, diagonal[cut], lower_here[cut], upper_here[cut])
        solution = solution[2:-2, 1:-1]
        direction = direction[2:-2, 1:-1]
        mask = inside[2 * sweep_index : inside.shape[0] - 2 * sweep_index, cut]
        residual = (residual[2:-2, 1:-1] - applied) * mask
        renewed = 1.0 / (2.0 * ratio_bound - factor)
        direction = renewed * factor * direction + 2.0 * renewed / spread * residual
        factor = renewed
    return solution + direction


def per_device(right_side, coupling, excess, metric):
    planes, radii, local_points = right_side.shape
    group_size = lax.axis_size("md")
    points = local_points * group_size
    local_radii = radii // group_size
    basis_table = fourier_table(points)
    lower_link, upper_link = links(coupling)
    gridded = lax.all_to_all(
        right_side.reshape(planes, group_size, local_radii, local_points),
        "md",
        split_axis=1,
        concat_axis=1,
        tiled=True,
    )
    spectral = jnp.dot(
        gridded.transpose(0, 2, 1, 3).reshape(planes * local_radii, points),
        basis_table,
        precision=lax.Precision.HIGHEST,
        preferred_element_type=jnp.float32,
    ).reshape(planes, local_radii, points)
    wavenumber = wave_numbers(points, points)
    fold = (points // 128, 128)
    spectral = spectral.reshape(planes, local_radii, *fold)
    plane_halo, radius_halo = 2 * SWEEPS, SWEEPS
    extended = with_halo(spectral, (("ax", 0),), plane_halo)
    extended = with_halo(extended, (("md", 1),), radius_halo)
    wide_radii = local_radii + 2 * radius_halo
    offset = lax.axis_index("md") * local_radii

    def around(values):
        padded = jnp.pad(values, (radius_halo, radius_halo + radii - values.shape[0]))
        return lax.dynamic_slice_in_dim(padded, offset, wide_radii)

    lower_here, upper_here = around(lower_link), around(upper_link)
    excess_here, metric_here = around(excess), around(metric)
    center, spread = bounds(lower_link, upper_link, excess, metric, wavenumber)
    diagonal = diagonal_terms(lower_here, upper_here, excess_here, metric_here, wavenumber)
    all_planes = planes * lax.axis_size("ax")
    plane_at = lax.axis_index("ax") * planes - plane_halo + jnp.arange(planes + 2 * plane_halo)
    radius_at = offset - radius_halo + jnp.arange(wide_radii)
    inside = (
        ((plane_at >= 0) & (plane_at < all_planes))[:, None]
        & ((radius_at >= 0) & (radius_at < radii))[None, :]
    ).astype(jnp.float32)[:, :, None, None]
    coefficients = (
        diagonal.reshape(wide_radii, *fold),
        lower_here[:, None, None],
        upper_here[:, None, None],
    )
    solution = chebyshev(
        extended, coefficients, inside, center.reshape(fold), spread.reshape(fold)
    )
    solved = jnp.dot(
        solution.reshape(planes * local_radii, points),
        basis_table.T,
        precision=lax.Precision.HIGHEST,
        preferred_element_type=jnp.float32,
    ).reshape(planes, local_radii, group_size, local_points).transpose(0, 2, 1, 3)
    returned = lax.all_to_all(solved, "md", split_axis=1, concat_axis=1, tiled=True)
    return returned.reshape(planes, radii, local_points)


def solution(mesh):
    return jax.shard_map(
        per_device,
        mesh=mesh,
        in_specs=(P("ax", None, "md"), P(), P(), P()),
        out_specs=P("ax", None, "md"),
        check_vma=False,
    )
```

```python
import math

import jax
import jax.numpy as jnp
from jax import lax
from jax.sharding import PartitionSpec as P

SWEEPS = 4


def with_halo(value, sides, width):
    for axis, dim in sides:
        size, length = (lax.axis_size(axis), value.shape[dim])
        up = [(i, (i + 1) % size) for i in range(size - 1)]
        down = [(j, i) for i, j in up]
        last = lax.slice_in_dim(value, length - width, length, axis=dim)
        leading = lax.slice_in_dim(value, 0, width, axis=dim)
        before = lax.ppermute(last, axis, up)
        after = lax.ppermute(leading, axis, down)
        value = jnp.concatenate([before, value, after], axis=dim)
    return value


def fourier_table(points):
    split = 32
    col_index = jnp.arange(points, dtype=jnp.int32)[None, :]
    middle = points // 2
    wavenumber = jnp.where(col_index <= middle, col_index, col_index - middle)
    scale = 2.0 * math.pi / points
    coarse = jnp.arange(points // split, dtype=jnp.int32)[:, None] * split
    fine = jnp.arange(split, dtype=jnp.int32)[:, None]
    coarse_angle = scale * ((coarse * wavenumber) % points).astype(jnp.float32)
    fine_angle = scale * ((fine * wavenumber) % points).astype(jnp.float32)
    ca, sa = jnp.cos(coarse_angle)[:, None, :], jnp.sin(coarse_angle)[:, None, :]
    cb, sb = jnp.cos(fine_angle)[None, :, :], jnp.sin(fine_angle)[None, :, :]
    weights = jnp.where(
        (col_index == 0) | (col_index == middle),
        jnp.float32(1.0 / points),
        jnp.float32(2.0 / points),
    )
    cosine = ca * cb - sa * sb
    sine = sa * cb + ca * sb
    basis_table = jnp.where(col_index[None] <= middle, cosine, sine).reshape(points, points)
    return lax.optimization_barrier(basis_table * jnp.sqrt(weights))


def wave_numbers(count, points):
    positions = jnp.arange(count, dtype=jnp.int32)
    middle = points // 2
    return jnp.where(positions <= middle, positions, positions - middle).astype(jnp.float32)


def links(coupling):
    zero_one = jnp.zeros((1,), coupling.dtype)
    return (jnp.concatenate([zero_one, coupling]), jnp.concatenate([coupling, zero_one]))


def bounds(lower_link, upper_link, excess, metric, wavenumber):
    squared = wavenumber * wavenumber
    radial_floor = excess[:, None] + metric[:, None] * squared[None, :]
    lowest = jnp.min(radial_floor, axis=0)
    highest = jnp.max(radial_floor + 2.0 * (lower_link + upper_link)[:, None], axis=0) + 16.0 / 3.0
    return ((highest + lowest) / 2.0, (highest - lowest) / 2.0)


def diagonal_terms(lower_here, upper_here, excess_here, metric_here, wavenumber):
    squared = wavenumber * wavenumber
    return (
        (lower_here + upper_here + excess_here)[:, None]
        + metric_here[:, None] * squared[None, :]
        + 2.5
    )


def apply_inner(direction, diagonal, lower_here, upper_here):
    middle = direction[2:-2, 1:-1]
    axial = 4.0 / 3.0 * (direction[1:-3, 1:-1] + direction[3:-1, 1:-1]) - 1.0 / 12.0 * (
        direction[:-4, 1:-1] + direction[4:, 1:-1]
    )
    radial = lower_here * direction[2:-2, :-2] + upper_here * direction[2:-2, 2:]
    return diagonal * middle - radial - axial


def chebyshev(source, coefficients, inside, center, spread):
    diagonal, lower_here, upper_here = coefficients
    ratio_bound = center / spread
    solution = jnp.zeros_like(source)
    residual = source
    direction = source / center
    factor = 1.0 / ratio_bound
    for sweep_index in range(1, SWEEPS + 1):
        solution = solution + direction
        cut = slice(sweep_index, diagonal.shape[0] - sweep_index)
        applied = apply_inner(direction, diagonal[cut], lower_here[cut], upper_here[cut])
        solution = solution[2:-2, 1:-1]
        direction = direction[2:-2, 1:-1]
        mask = inside[2 * sweep_index : inside.shape[0] - 2 * sweep_index, cut]
        residual = (residual[2:-2, 1:-1] - applied) * mask
        renewed = 1.0 / (2.0 * ratio_bound - factor)
        direction = renewed * factor * direction + 2.0 * renewed / spread * residual
        factor = renewed
    return solution + direction


def per_device(right_side, coupling, excess, metric):
    planes, radii, local_points = right_side.shape
    group_size = lax.axis_size("md")
    points = local_points * group_size
    local_radii = radii // group_size
    basis_table = fourier_table(points)
    lower_link, upper_link = links(coupling)
    gridded = lax.all_to_all(
        right_side.reshape(planes, group_size, local_radii, local_points),
        "md",
        split_axis=1,
        concat_axis=1,
        tiled=True,
    )
    fold = (points // 128, 128)
    spectral = lax.dot_general(
        gridded.transpose(0, 2, 1, 3).reshape(planes * local_radii, points),
        basis_table.reshape(points, *fold),
        (((1,), (0,)), ((), ())),
        precision=lax.Precision.HIGHEST,
        preferred_element_type=jnp.float32,
    ).reshape(planes, local_radii, *fold)
    wavenumber = wave_numbers(points, points)
    plane_halo, radius_halo = 2 * SWEEPS, SWEEPS
    extended = with_halo(spectral, (("ax", 0),), plane_halo)
    extended = with_halo(extended, (("md", 1),), radius_halo)
    wide_radii = local_radii + 2 * radius_halo
    offset = lax.axis_index("md") * local_radii

    def around(values):
        padded = jnp.pad(values, (radius_halo, radius_halo + radii - values.shape[0]))
        return lax.dynamic_slice_in_dim(padded, offset, wide_radii)

    lower_here, upper_here = around(lower_link), around(upper_link)
    excess_here, metric_here = around(excess), around(metric)
    center, spread = bounds(lower_link, upper_link, excess, metric, wavenumber)
    diagonal = diagonal_terms(lower_here, upper_here, excess_here, metric_here, wavenumber)
    all_planes = planes * lax.axis_size("ax")
    plane_at = lax.axis_index("ax") * planes - plane_halo + jnp.arange(planes + 2 * plane_halo)
    radius_at = offset - radius_halo + jnp.arange(wide_radii)
    inside = (
        ((plane_at >= 0) & (plane_at < all_planes))[:, None]
        & ((radius_at >= 0) & (radius_at < radii))[None, :]
    ).astype(jnp.float32)[:, :, None, None]
    coefficients = (
        diagonal.reshape(wide_radii, *fold),
        lower_here[:, None, None],
        upper_here[:, None, None],
    )
    solution = chebyshev(
        extended, coefficients, inside, center.reshape(fold), spread.reshape(fold)
    )
    solved = lax.dot_general(
        solution.reshape(planes * local_radii, *fold),
        basis_table.reshape(points, *fold),
        (((1, 2), (1, 2)), ((), ())),
        precision=lax.Precision.HIGH,
        preferred_element_type=jnp.float32,
    ).reshape(planes, local_radii, group_size, local_points).transpose(0, 2, 1, 3)
    returned = lax.all_to_all(solved, "md", split_axis=1, concat_axis=1, tiled=True)
    return returned.reshape(planes, radii, local_points)


def solution(mesh):
    return jax.shard_map(
        per_device,
        mesh=mesh,
        in_specs=(P("ax", None, "md"), P(), P(), P()),
        out_specs=P("ax", None, "md"),
        check_vma=False,
    )
```

```python
import math

import jax
import jax.numpy as jnp
from jax import lax
from jax.sharding import PartitionSpec as P

SWEEPS = 4


def with_halo(value, sides, width):
    for axis, dim in sides:
        size, length = (lax.axis_size(axis), value.shape[dim])
        up = [(i, (i + 1) % size) for i in range(size - 1)]
        down = [(j, i) for i, j in up]
        last = lax.slice_in_dim(value, length - width, length, axis=dim)
        leading = lax.slice_in_dim(value, 0, width, axis=dim)
        before = lax.ppermute(last, axis, up)
        after = lax.ppermute(leading, axis, down)
        value = jnp.concatenate([before, value, after], axis=dim)
    return value


def fourier_table(points):
    split = 32
    col_index = jnp.arange(points, dtype=jnp.int32)[None, :]
    middle = points // 2
    wavenumber = jnp.where(col_index <= middle, col_index, col_index - middle)
    scale = 2.0 * math.pi / points
    coarse = jnp.arange(points // split, dtype=jnp.int32)[:, None] * split
    fine = jnp.arange(split, dtype=jnp.int32)[:, None]
    coarse_angle = scale * ((coarse * wavenumber) % points).astype(jnp.float32)
    fine_angle = scale * ((fine * wavenumber) % points).astype(jnp.float32)
    ca, sa = jnp.cos(coarse_angle)[:, None, :], jnp.sin(coarse_angle)[:, None, :]
    cb, sb = jnp.cos(fine_angle)[None, :, :], jnp.sin(fine_angle)[None, :, :]
    weights = jnp.where(
        (col_index == 0) | (col_index == middle),
        jnp.float32(1.0 / points),
        jnp.float32(2.0 / points),
    )
    cosine = ca * cb - sa * sb
    sine = sa * cb + ca * sb
    basis_table = jnp.where(col_index[None] <= middle, cosine, sine).reshape(points, points)
    return lax.optimization_barrier(basis_table * jnp.sqrt(weights))


def wave_numbers(count, points):
    positions = jnp.arange(count, dtype=jnp.int32)
    middle = points // 2
    return jnp.where(positions <= middle, positions, positions - middle).astype(jnp.float32)


def links(coupling):
    zero_one = jnp.zeros((1,), coupling.dtype)
    return (jnp.concatenate([zero_one, coupling]), jnp.concatenate([coupling, zero_one]))


def bounds(lower_link, upper_link, excess, metric, wavenumber):
    squared = wavenumber * wavenumber
    radial_floor = excess[:, None] + metric[:, None] * squared[None, :]
    lowest = jnp.min(radial_floor, axis=0)
    highest = jnp.max(radial_floor + 2.0 * (lower_link + upper_link)[:, None], axis=0) + 16.0 / 3.0
    return ((highest + lowest) / 2.0, (highest - lowest) / 2.0)


def diagonal_terms(lower_here, upper_here, excess_here, metric_here, wavenumber):
    squared = wavenumber * wavenumber
    return (
        (lower_here + upper_here + excess_here)[:, None]
        + metric_here[:, None] * squared[None, :]
        + 2.5
    )


def apply_inner(direction, diagonal, lower_here, upper_here):
    middle = direction[2:-2, 1:-1]
    axial = 4.0 / 3.0 * (direction[1:-3, 1:-1] + direction[3:-1, 1:-1]) - 1.0 / 12.0 * (
        direction[:-4, 1:-1] + direction[4:, 1:-1]
    )
    radial = lower_here * direction[2:-2, :-2] + upper_here * direction[2:-2, 2:]
    return diagonal * middle - radial - axial


def chebyshev(source, coefficients, inside, center, spread):
    diagonal, lower_here, upper_here = coefficients
    ratio_bound = center / spread
    solution = jnp.zeros_like(source)
    residual = source
    direction = source / center
    factor = 1.0 / ratio_bound
    for sweep_index in range(1, SWEEPS + 1):
        solution = solution + direction
        cut = slice(sweep_index, diagonal.shape[0] - sweep_index)
        applied = apply_inner(direction, diagonal[cut], lower_here[cut], upper_here[cut])
        solution = solution[2:-2, 1:-1]
        direction = direction[2:-2, 1:-1]
        mask = inside[2 * sweep_index : inside.shape[0] - 2 * sweep_index, cut]
        residual = (residual[2:-2, 1:-1] - applied) * mask
        renewed = 1.0 / (2.0 * ratio_bound - factor)
        direction = renewed * factor * direction + 2.0 * renewed / spread * residual
        factor = renewed
    return solution + direction


def per_device(right_side, coupling, excess, metric):
    planes, radii, local_points = right_side.shape
    group_size = lax.axis_size("md")
    points = local_points * group_size
    local_radii = radii // group_size
    basis_table = fourier_table(points)
    lower_link, upper_link = links(coupling)
    gridded = lax.all_to_all(
        right_side.reshape(planes, group_size, local_radii, local_points),
        "md",
        split_axis=1,
        concat_axis=1,
        tiled=True,
    )
    fold = (points // 128, 128)
    spectral = lax.dot_general(
        gridded.transpose(0, 2, 1, 3).reshape(planes * local_radii, points),
        basis_table.reshape(points, *fold),
        (((1,), (0,)), ((), ())),
        precision=lax.Precision.HIGHEST,
        preferred_element_type=jnp.float32,
    ).reshape(planes, local_radii, *fold)
    wavenumber = wave_numbers(points, points)
    plane_halo, radius_halo = 2 * SWEEPS, SWEEPS
    extended = with_halo(spectral, (("ax", 0),), plane_halo)
    extended = with_halo(extended, (("md", 1),), radius_halo)
    wide_radii = local_radii + 2 * radius_halo
    offset = lax.axis_index("md") * local_radii

    def around(values):
        padded = jnp.pad(values, (radius_halo, radius_halo + radii - values.shape[0]))
        return lax.dynamic_slice_in_dim(padded, offset, wide_radii)

    lower_here, upper_here = around(lower_link), around(upper_link)
    excess_here, metric_here = around(excess), around(metric)
    center, spread = bounds(lower_link, upper_link, excess, metric, wavenumber)
    diagonal = diagonal_terms(lower_here, upper_here, excess_here, metric_here, wavenumber)
    all_planes = planes * lax.axis_size("ax")
    plane_at = lax.axis_index("ax") * planes - plane_halo + jnp.arange(planes + 2 * plane_halo)
    radius_at = offset - radius_halo + jnp.arange(wide_radii)
    inside = (
        ((plane_at >= 0) & (plane_at < all_planes))[:, None]
        & ((radius_at >= 0) & (radius_at < radii))[None, :]
    ).astype(jnp.float32)[:, :, None, None]
    coefficients = (
        diagonal.reshape(wide_radii, *fold),
        lower_here[:, None, None],
        upper_here[:, None, None],
    )
    solution = chebyshev(
        extended, coefficients, inside, center.reshape(fold), spread.reshape(fold)
    )
    halves = []
    for part in (slice(0, planes // 2), slice(planes // 2, planes)):
        solved = lax.dot_general(
            solution[part].reshape(planes // 2 * local_radii, *fold),
            basis_table.reshape(points, *fold),
            (((1, 2), (1, 2)), ((), ())),
            precision=lax.Precision.HIGH,
            preferred_element_type=jnp.float32,
        ).reshape(planes // 2, local_radii, group_size, local_points).transpose(0, 2, 1, 3)
        halves.append(lax.all_to_all(solved, "md", split_axis=1, concat_axis=1, tiled=True))
    returned = jnp.concatenate(halves, axis=0)
    return returned.reshape(planes, radii, local_points)


def solution(mesh):
    return jax.shard_map(
        per_device,
        mesh=mesh,
        in_specs=(P("ax", None, "md"), P(), P(), P()),
        out_specs=P("ax", None, "md"),
        check_vma=False,
    )
```

```python
import math

import jax
import jax.numpy as jnp
from jax import lax
from jax.sharding import PartitionSpec as P

SWEEPS = 4


def with_halo(value, sides, width):
    for axis, dim in sides:
        size, length = (lax.axis_size(axis), value.shape[dim])
        up = [(i, (i + 1) % size) for i in range(size - 1)]
        down = [(j, i) for i, j in up]
        last = lax.slice_in_dim(value, length - width, length, axis=dim)
        leading = lax.slice_in_dim(value, 0, width, axis=dim)
        before = lax.ppermute(last, axis, up)
        after = lax.ppermute(leading, axis, down)
        value = jnp.concatenate([before, value, after], axis=dim)
    return value


def fourier_table(points):
    split = 32
    col_index = jnp.arange(points, dtype=jnp.int32)[None, :]
    middle = points // 2
    wavenumber = jnp.where(col_index <= middle, col_index, col_index - middle)
    scale = 2.0 * math.pi / points
    coarse = jnp.arange(points // split, dtype=jnp.int32)[:, None] * split
    fine = jnp.arange(split, dtype=jnp.int32)[:, None]
    coarse_angle = scale * ((coarse * wavenumber) % points).astype(jnp.float32)
    fine_angle = scale * ((fine * wavenumber) % points).astype(jnp.float32)
    ca, sa = jnp.cos(coarse_angle)[:, None, :], jnp.sin(coarse_angle)[:, None, :]
    cb, sb = jnp.cos(fine_angle)[None, :, :], jnp.sin(fine_angle)[None, :, :]
    weights = jnp.where(
        (col_index == 0) | (col_index == middle),
        jnp.float32(1.0 / points),
        jnp.float32(2.0 / points),
    )
    cosine = ca * cb - sa * sb
    sine = sa * cb + ca * sb
    basis_table = jnp.where(col_index[None] <= middle, cosine, sine).reshape(points, points)
    return lax.optimization_barrier(basis_table * jnp.sqrt(weights))


def wave_numbers(count, points):
    positions = jnp.arange(count, dtype=jnp.int32)
    middle = points // 2
    return jnp.where(positions <= middle, positions, positions - middle).astype(jnp.float32)


def links(coupling):
    zero_one = jnp.zeros((1,), coupling.dtype)
    return (jnp.concatenate([zero_one, coupling]), jnp.concatenate([coupling, zero_one]))


def bounds(lower_link, upper_link, excess, metric, wavenumber):
    squared = wavenumber * wavenumber
    radial_floor = excess[:, None] + metric[:, None] * squared[None, :]
    lowest = jnp.min(radial_floor, axis=0)
    highest = jnp.max(radial_floor + 2.0 * (lower_link + upper_link)[:, None], axis=0) + 16.0 / 3.0
    return ((highest + lowest) / 2.0, (highest - lowest) / 2.0)


def diagonal_terms(lower_here, upper_here, excess_here, metric_here, wavenumber):
    squared = wavenumber * wavenumber
    return (
        (lower_here + upper_here + excess_here)[:, None]
        + metric_here[:, None] * squared[None, :]
        + 2.5
    )


def apply_inner(direction, diagonal, lower_here, upper_here):
    middle = direction[2:-2, 1:-1]
    axial = 4.0 / 3.0 * (direction[1:-3, 1:-1] + direction[3:-1, 1:-1]) - 1.0 / 12.0 * (
        direction[:-4, 1:-1] + direction[4:, 1:-1]
    )
    radial = lower_here * direction[2:-2, :-2] + upper_here * direction[2:-2, 2:]
    return diagonal * middle - radial - axial


def chebyshev(source, coefficients, inside, center, spread):
    diagonal, lower_here, upper_here = coefficients
    ratio_bound = center / spread
    solution = jnp.zeros_like(source)
    residual = source
    direction = source / center
    factor = 1.0 / ratio_bound
    for sweep_index in range(1, SWEEPS + 1):
        solution = solution + direction
        cut = slice(sweep_index, diagonal.shape[0] - sweep_index)
        applied = apply_inner(direction, diagonal[cut], lower_here[cut], upper_here[cut])
        solution = solution[2:-2, 1:-1]
        direction = direction[2:-2, 1:-1]
        mask = inside[2 * sweep_index : inside.shape[0] - 2 * sweep_index, cut]
        residual = (residual[2:-2, 1:-1] - applied) * mask
        renewed = 1.0 / (2.0 * ratio_bound - factor)
        direction = renewed * factor * direction + 2.0 * renewed / spread * residual
        factor = renewed
    return solution + direction


def per_device(right_side, coupling, excess, metric):
    planes, radii, local_points = right_side.shape
    group_size = lax.axis_size("md")
    points = local_points * group_size
    local_radii = radii // group_size
    basis_table = fourier_table(points)
    lower_link, upper_link = links(coupling)
    gridded = lax.all_to_all(
        right_side.reshape(planes, group_size, local_radii, local_points),
        "md",
        split_axis=1,
        concat_axis=1,
        tiled=True,
    )
    fold = (points // 128, 128)
    spectral = lax.dot_general(
        gridded,
        basis_table.reshape(group_size, local_points, *fold),
        (((1, 3), (0, 1)), ((), ())),
        precision=lax.Precision.HIGHEST,
        preferred_element_type=jnp.float32,
    ).reshape(planes, local_radii, *fold)
    wavenumber = wave_numbers(points, points)
    plane_halo, radius_halo = 2 * SWEEPS, SWEEPS
    extended = with_halo(spectral, (("ax", 0),), plane_halo)
    extended = with_halo(extended, (("md", 1),), radius_halo)
    wide_radii = local_radii + 2 * radius_halo
    offset = lax.axis_index("md") * local_radii

    def around(values):
        padded = jnp.pad(values, (radius_halo, radius_halo + radii - values.shape[0]))
        return lax.dynamic_slice_in_dim(padded, offset, wide_radii)

    lower_here, upper_here = around(lower_link), around(upper_link)
    excess_here, metric_here = around(excess), around(metric)
    center, spread = bounds(lower_link, upper_link, excess, metric, wavenumber)
    diagonal = diagonal_terms(lower_here, upper_here, excess_here, metric_here, wavenumber)
    all_planes = planes * lax.axis_size("ax")
    plane_at = lax.axis_index("ax") * planes - plane_halo + jnp.arange(planes + 2 * plane_halo)
    radius_at = offset - radius_halo + jnp.arange(wide_radii)
    inside = (
        ((plane_at >= 0) & (plane_at < all_planes))[:, None]
        & ((radius_at >= 0) & (radius_at < radii))[None, :]
    ).astype(jnp.float32)[:, :, None, None]
    coefficients = (
        diagonal.reshape(wide_radii, *fold),
        lower_here[:, None, None],
        upper_here[:, None, None],
    )
    solution = chebyshev(
        extended, coefficients, inside, center.reshape(fold), spread.reshape(fold)
    )
    solved = lax.dot_general(
        solution.reshape(planes * local_radii, *fold),
        basis_table.reshape(points, *fold),
        (((1, 2), (1, 2)), ((), ())),
        precision=lax.Precision.HIGH,
        preferred_element_type=jnp.float32,
    ).reshape(planes, local_radii, group_size, local_points).transpose(0, 2, 1, 3)
    returned = lax.all_to_all(solved, "md", split_axis=1, concat_axis=1, tiled=True)
    return returned.reshape(planes, radii, local_points)


def solution(mesh):
    return jax.shard_map(
        per_device,
        mesh=mesh,
        in_specs=(P("ax", None, "md"), P(), P(), P()),
        out_specs=P("ax", None, "md"),
        check_vma=False,
    )
```
